32 devices in a mesh: param: 4 (over y, core), ex: 8 (over z, x).
Axes of the slice: x: 2, y: 2, z: 4, core: 2. Of those that a mesh axis runs over, the one named last changes fastest.
Arguments:
- activations: bfloat16 [32, 128, 8192], P('ex', None, 'param'), may hold values from -6 to 6
- out_grads: bfloat16 [32, 128, 8192], P('ex', None, 'param'), may hold values from -6 to 6
- proj_in: bfloat16 [8192, 32], P('param'), may hold values from -0.0625 to 0.0625
- proj_out: bfloat16 [8192, 32], P('param'), may hold values from -0.0625 to 0.0625
- prior: float32 [1024, 1024], P('ex', 'param'), as said below
- probes: bfloat16 [512, 1024], P(('param', 'ex')), may hold values from -6 to 6
Outputs:
- scores: float32 [512, 32], P('param', 'ex')
The draws below stay inside these ranges and needn't reach their ends.
Inputs may be any that keep to these rules, and one draw needn't show every extreme that they name: prior is symmetric positive definite with smallest eigenvalue at least 0.1.
All inputs are finite; a program needn't handle non-finite values.
Results may differ from the reference program's by a relative error of at most 0.0042.
Values may be sent and summed in bfloat16 or wider, within the bound.
No kernel may reach another device: no remote copies, remote signals or barrier semaphores. Data moves between devices by JAX's collectives and lax.ppermute only.
A program may use at most 64 MiB of HBM per device.

```python
import math
import jax
import jax.numpy as jnp
from jax import lax

D = 8192
TOK = 128
K_IN = 32
K_OUT = 32
FEAT = 1024
TRAIN = 32
PROBES = 512


def draw_prior(key, part):
    factor_key = jax.random.fold_in(key, 11)
    damp_key = jax.random.fold_in(key, 12)
    weight_key = jax.random.fold_in(key, 14)
    entries = jax.random.randint(factor_key, (FEAT, FEAT), -2, 3, jnp.int32)
    powers = jax.random.randint(weight_key, (FEAT,), 0, 11, jnp.int32)
    row_weights = jnp.left_shift(jnp.ones((FEAT,), jnp.int32), powers)
    weighted = entries * row_weights[:, None]
    weighted_gram = lax.dot_general(weighted, entries, (((0,), (0,)), ((), ())), preferred_element_type=jnp.int32)
    scaled = weighted_gram.astype(jnp.float32) * (0.1 / FEAT)
    damping = jax.random.uniform(damp_key, (FEAT,), jnp.float32, 0.1, 0.5)
    identity = jnp.eye(FEAT, dtype=jnp.float32)
    return scaled + identity * damping[None, :]


def level_of(stream_key, extent, shards, smallest, high):
    gain, own = 1.0, jax.random.fold_in(stream_key, 6)
    for dim, blocks in shards:
        steps = jnp.exp(jax.random.uniform(jax.random.fold_in(own, dim), (blocks,), jnp.float32, smallest / len(shards), high / len(shards)))
        gain = gain * jnp.repeat(steps, extent[dim] // blocks).reshape([-1 if axis == dim else 1 for axis in range(len(extent))])
    return gain


def gaussian(rng, dims, spread, bound, shards=(), kind=jnp.bfloat16):
    result = spread * jax.random.normal(rng, dims, jnp.float32)
    if shards:
        result = result * level_of(rng, dims, shards, -0.22, 0.18)
    return jnp.clip(result, -bound, bound).astype(kind)


def setup_inputs(seed: int = 0) -> dict:
    arg_keys = jax.random.split(jax.random.key(seed), 7)
    return {
        "activations": gaussian(arg_keys[0], (TRAIN, TOK, D), 1.0, 6.0, ((0, 8), (2, 4))),
        "out_grads": gaussian(arg_keys[1], (TRAIN, TOK, D), 1.0, 6.0, ((0, 8), (2, 4))),
        "proj_in": gaussian(arg_keys[2], (D, K_IN), D ** -0.5, 0.0625, ((0, 4),)),
        "proj_out": gaussian(arg_keys[3], (D, K_OUT), D ** -0.5, 0.0625, ((0, 4),)),
        "prior": draw_prior(jax.random.fold_in(arg_keys[6], 71), 0),
        "probes": gaussian(arg_keys[5], (PROBES, FEAT), 1.0, 6.0, ((0, 32),)),
    }


def reference(activations, out_grads, proj_in, proj_out, prior, probes):
    token_scale = 1.0 / math.sqrt(TOK)

    def one_example(pair):
        acts, grads = pair
        first = jnp.dot(acts.astype(jnp.float32), proj_in.astype(jnp.float32), preferred_element_type=jnp.float32)
        second = jnp.dot(grads.astype(jnp.float32), proj_out.astype(jnp.float32), preferred_element_type=jnp.float32)
        outer_prod = jnp.dot(second.T, first, precision=lax.Precision.HIGHEST)
        return (outer_prod * token_scale).reshape(-1).astype(jnp.bfloat16)
    features = lax.map(one_example, (activations, out_grads))
    kernel = prior + jnp.dot(features.T.astype(jnp.float32), features.astype(jnp.float32), preferred_element_type=jnp.float32) / TRAIN
    lower = jnp.linalg.cholesky(kernel)
    halfway = lax.linalg.triangular_solve(lower, features.astype(jnp.float32).T, left_side=True, lower=True)
    solved_t = lax.linalg.triangular_solve(lower, halfway, left_side=True, lower=True, transpose_a=True)
    solved = solved_t.T.astype(jnp.bfloat16)
    feat_scale = 1.0 / math.sqrt(FEAT)
    return jnp.dot(probes.astype(jnp.float32), solved.T.astype(jnp.float32), preferred_element_type=jnp.float32) * feat_scale
```

```python
import math

import jax
import jax.numpy as jnp
from jax import lax
from jax.sharding import PartitionSpec as P


def outer_terms(factors, in_width):
    first = factors[:, :in_width]
    second = factors[:, in_width:]
    product = jnp.einsum("eol,eil->eoi", second, first, precision=lax.Precision.HIGHEST)
    return product.reshape(product.shape[0], -1)


def spd_solve(matrix, rhs_t):
    lower_factor = jnp.linalg.cholesky(matrix)
    halfway = lax.linalg.triangular_solve(lower_factor, rhs_t, left_side=True, lower=True)
    return lax.linalg.triangular_solve(
        lower_factor, halfway, left_side=True, lower=True, transpose_a=True
    )


def gather_prior(prior):
    n_ex = lax.axis_size("ex")
    n_par = lax.axis_size("param")
    rows, cols = prior.shape
    blocks = lax.all_gather(prior, ("ex", "param"), axis=0, tiled=False)
    blocks = blocks.reshape(n_ex, n_par, rows, cols).transpose(0, 2, 1, 3)
    return blocks.reshape(n_ex * rows, n_par * cols)


def per_device(activations, out_grads, proj_in, proj_out, prior, probes):
    full_prior = gather_prior(prior)
    tokens = activations.shape[1]
    in_width = proj_in.shape[1]
    factor_in = jnp.einsum("eld,dk->ekl", activations, proj_in, preferred_element_type=jnp.float32)
    factor_out = jnp.einsum("eld,dk->ekl", out_grads, proj_out, preferred_element_type=jnp.float32)
    factors = jnp.concatenate((factor_in, factor_out), axis=1)
    factors = lax.psum(factors, "param")
    summed = outer_terms(factors, in_width)
    features = (summed * (1.0 / math.sqrt(tokens))).astype(jnp.bfloat16)
    local_count, feat_dim = features.shape
    all_features = lax.all_gather(features.astype(jnp.float32), "ex", axis=0, tiled=True)
    train_count = all_features.shape[0]
    prior_solved_t = spd_solve(full_prior, all_features.T)
    gram = jnp.dot(all_features, prior_solved_t, precision=lax.Precision.HIGHEST)
    small = gram + train_count * jnp.eye(train_count, dtype=jnp.float32)
    solved_all = (train_count * spd_solve(small, prior_solved_t.T)).astype(jnp.bfloat16)
    row_start = lax.axis_index("ex") * local_count
    solved = lax.dynamic_slice_in_dim(solved_all, row_start, local_count, 0)
    inverse_root = 1.0 / math.sqrt(feat_dim)
    return (
        jnp.dot(
            lax.all_gather(probes.astype(jnp.float32), "ex", axis=0, tiled=True).astype(jnp.bfloat16),
            solved.T,
            preferred_element_type=jnp.float32,
        )
        * inverse_root
    )


def solution(mesh):
    return jax.shard_map(
        per_device,
        mesh=mesh,
        in_specs=(
            P("ex", None, "param"),
            P("ex", None, "param"),
            P("param", None),
            P("param", None),
            P("ex", "param"),
            P(("param", "ex"), None),
        ),
        out_specs=P("param", "ex"),
        check_vma=False,
    )
```

```python
import math

import jax
import jax.numpy as jnp
from jax import lax
from jax.sharding import PartitionSpec as P


def outer_terms(factors, in_width):
    first = factors[:, :in_width]
    second = factors[:, in_width:]
    product = jnp.einsum("eol,eil->eoi", second, first, precision=lax.Precision.HIGHEST)
    return product.reshape(product.shape[0], -1)


def spd_solve(matrix, rhs_t):
    lower_factor = jnp.linalg.cholesky(matrix)
    halfway = lax.linalg.triangular_solve(lower_factor, rhs_t, left_side=True, lower=True)
    return lax.linalg.triangular_solve(
        lower_factor, halfway, left_side=True, lower=True, transpose_a=True
    )


def mm(a, b):
    return jnp.dot(a, b, precision=lax.Precision.HIGHEST, preferred_element_type=jnp.float32)


def blocked_cholesky(matrix, block):
    count = matrix.shape[0] // block
    eye = jnp.eye(block, dtype=jnp.float32)
    inverses, panels = [], []
    trailing = matrix
    for k in range(count):
        diag = lax.linalg.cholesky(trailing[:block, :block], symmetrize_input=False)
        inverse = lax.linalg.triangular_solve(diag, eye, left_side=True, lower=True)
        inverses.append(inverse)
        if k + 1 < count:
            panel = mm(trailing[block:, :block], inverse.T)
            panels.append(panel)
            trailing = trailing[block:, block:] - mm(panel, panel.T)
    return inverses, panels


def blocked_solve(inverses, panels, rhs, block):
    count = len(inverses)
    parts = []
    rest = rhs
    for k in range(count):
        part = mm(inverses[k], rest[:block])
        parts.append(part)
        if k + 1 < count:
            rest = rest[block:] - mm(panels[k], part)
    done = None
    for k in reversed(range(count)):
        target = parts[k]
        if done is not None:
            target = target - mm(panels[k].T, done)
        part = mm(inverses[k].T, target)
        done = part if done is None else jnp.concatenate((part, done), axis=0)
    return done


def gather_rows(block_rows, axis_name):
    count = lax.axis_size(axis_name)
    rows = block_rows.shape[0]
    padded = jnp.zeros((count * rows,) + block_rows.shape[1:], block_rows.dtype)
    padded = lax.dynamic_update_slice_in_dim(padded, block_rows, lax.axis_index(axis_name) * rows, 0)
    return lax.psum(padded, axis_name)


def gather_prior(prior):
    n_ex = lax.axis_size("ex")
    n_par = lax.axis_size("param")
    rows, cols = prior.shape
    blocks = lax.all_gather(prior, ("ex", "param"), axis=0, tiled=False)
    blocks = blocks.reshape(n_ex, n_par, rows, cols).transpose(0, 2, 1, 3)
    return blocks.reshape(n_ex * rows, n_par * cols)


def per_device(activations, out_grads, proj_in, proj_out, prior, probes):
    full_prior = gather_prior(prior)
    tokens = activations.shape[1]
    in_width = proj_in.shape[1]
    factor_in = jnp.einsum("eld,dk->ekl", activations, proj_in, preferred_element_type=jnp.float32)
    factor_out = jnp.einsum("eld,dk->ekl", out_grads, proj_out, preferred_element_type=jnp.float32)
    factors = jnp.concatenate((factor_in, factor_out), axis=1)
    factors = lax.psum(factors, "param")
    summed = outer_terms(factors, in_width)
    features = (summed * (1.0 / math.sqrt(tokens))).astype(jnp.bfloat16)
    local_count, feat_dim = features.shape
    all_features = gather_rows(features.astype(jnp.float32), "ex")
    train_count = all_features.shape[0]
    block = 128 if feat_dim % 128 == 0 else feat_dim
    inverses, panels = blocked_cholesky(full_prior, block)
    prior_solved_t = blocked_solve(inverses, panels, all_features.T, block)
    gram = jnp.dot(all_features, prior_solved_t, precision=lax.Precision.HIGHEST)
    small = gram + train_count * jnp.eye(train_count, dtype=jnp.float32)
    solved_all = (train_count * spd_solve(small, prior_solved_t.T)).astype(jnp.bfloat16)
    row_start = lax.axis_index("ex") * local_count
    solved = lax.dynamic_slice_in_dim(solved_all, row_start, local_count, 0)
    inverse_root = 1.0 / math.sqrt(feat_dim)
    block_probes = gather_rows(probes.astype(jnp.float32), "ex")
    return mm(block_probes, solved.astype(jnp.float32).T) * inverse_root


def solution(mesh):
    return jax.shard_map(
        per_device,
        mesh=mesh,
        in_specs=(
            P("ex", None, "param"),
            P("ex", None, "param"),
            P("param", None),
            P("param", None),
            P("ex", "param"),
            P(("param", "ex"), None),
        ),
        out_specs=P("param", "ex"),
        check_vma=False,
    )
```

```python
import math

import jax
import jax.numpy as jnp
from jax import lax
from jax.experimental import pallas as pl
from jax.experimental.pallas import tpu as pltpu
from jax.sharding import PartitionSpec as P


def _inverse_factor_kernel(a_ref, w_ref, s_ref):
    n = a_ref.shape[0]
    s_ref[...] = a_ref[...]
    rows = lax.broadcasted_iota(jnp.int32, (n, n), 0)
    cols = lax.broadcasted_iota(jnp.int32, (n, n), 1)
    w_ref[...] = jnp.where(rows == cols, 1.0, 0.0).astype(jnp.float32)
    for group in range(n // 8):
        low = group * 8

        def step(t, carry):
            j = low + t
            pivot_row = s_ref[pl.ds(j, 1), :]
            inverse_row = w_ref[pl.ds(j, 1), :]
            lane = lax.broadcasted_iota(jnp.int32, (1, n), 1)
            pivot = jnp.sum(jnp.where(lane == j, pivot_row, 0.0), axis=1, keepdims=True)
            scale = 1.0 / jnp.sqrt(pivot)
            pivot_row = pivot_row * scale
            inverse_row = inverse_row * scale
            rest = s_ref[low:, :]
            lanes = lax.broadcasted_iota(jnp.int32, rest.shape, 1)
            column = jnp.sum(jnp.where(lanes == j, rest, 0.0), axis=1, keepdims=True)
            below = lax.broadcasted_iota(jnp.int32, (n - low, 1), 0) + low
            factor = jnp.where(below > j, column * scale, 0.0)
            s_ref[low:, :] = rest - factor * pivot_row
            w_ref[low:, :] = w_ref[low:, :] - factor * inverse_row
            s_ref[pl.ds(j, 1), :] = pivot_row
            w_ref[pl.ds(j, 1), :] = inverse_row
            return carry

        lax.fori_loop(0, 8, step, 0)


def inverse_factor(block):
    n = block.shape[0]
    return pl.pallas_call(
        _inverse_factor_kernel,
        out_shape=jax.ShapeDtypeStruct((n, n), jnp.float32),
        in_specs=[pl.BlockSpec(memory_space=pltpu.VMEM)],
        out_specs=pl.BlockSpec(memory_space=pltpu.VMEM),
        scratch_shapes=[pltpu.VMEM((n, n), jnp.float32)],
    )(block)


def outer_terms(factors, in_width):
    first = factors[:, :in_width]
    second = factors[:, in_width:]
    product = jnp.einsum("eol,eil->eoi", second, first, precision=lax.Precision.HIGHEST)
    return product.reshape(product.shape[0], -1)


def spd_solve(matrix, rhs_t):
    lower_factor = jnp.linalg.cholesky(matrix)
    halfway = lax.linalg.triangular_solve(lower_factor, rhs_t, left_side=True, lower=True)
    return lax.linalg.triangular_solve(
        lower_factor, halfway, left_side=True, lower=True, transpose_a=True
    )


def mm(a, b):
    return jnp.dot(a, b, precision=lax.Precision.HIGHEST, preferred_element_type=jnp.float32)


def blocked_cholesky(matrix, block):
    count = matrix.shape[0] // block
    inverses, panels = [], []
    trailing = matrix
    for k in range(count):
        inverse = inverse_factor(trailing[:block, :block])
        inverses.append(inverse)
        if k + 1 < count:
            panel = mm(trailing[block:, :block], inverse.T)
            panels.append(panel)
            trailing = trailing[block:, block:] - mm(panel, panel.T)
    return inverses, panels


def blocked_solve(inverses, panels, rhs, block):
    count = len(inverses)
    parts = []
    rest = rhs
    for k in range(count):
        part = mm(inverses[k], rest[:block])
        parts.append(part)
        if k + 1 < count:
            rest = rest[block:] - mm(panels[k], part)
    done = None
    for k in reversed(range(count)):
        target = parts[k]
        if done is not None:
            target = target - mm(panels[k].T, done)
        part = mm(inverses[k].T, target)
        done = part if done is None else jnp.concatenate((part, done), axis=0)
    return done


def gather_rows(block_rows, axis_name):
    count = lax.axis_size(axis_name)
    rows = block_rows.shape[0]
    padded = jnp.zeros((count * rows,) + block_rows.shape[1:], block_rows.dtype)
    padded = lax.dynamic_update_slice_in_dim(padded, block_rows, lax.axis_index(axis_name) * rows, 0)
    return lax.psum(padded, axis_name)


def gather_prior(prior):
    n_ex = lax.axis_size("ex")
    n_par = lax.axis_size("param")
    rows, cols = prior.shape
    blocks = lax.all_gather(prior, ("ex", "param"), axis=0, tiled=False)
    blocks = blocks.reshape(n_ex, n_par, rows, cols).transpose(0, 2, 1, 3)
    return blocks.reshape(n_ex * rows, n_par * cols)


def per_device(activations, out_grads, proj_in, proj_out, prior, probes):
    full_prior = gather_prior(prior)
    tokens = activations.shape[1]
    in_width = proj_in.shape[1]
    factor_in = jnp.einsum("eld,dk->ekl", activations, proj_in, preferred_element_type=jnp.float32)
    factor_out = jnp.einsum("eld,dk->ekl", out_grads, proj_out, preferred_element_type=jnp.float32)
    factors = jnp.concatenate((factor_in, factor_out), axis=1)
    factors = lax.psum(factors, "param")
    summed = outer_terms(factors, in_width)
    features = (summed * (1.0 / math.sqrt(tokens))).astype(jnp.bfloat16)
    local_count, feat_dim = features.shape
    all_features = gather_rows(features.astype(jnp.float32), "ex")
    train_count = all_features.shape[0]
    block = 128 if feat_dim % 128 == 0 else feat_dim
    inverses, panels = blocked_cholesky(full_prior, block)
    prior_solved_t = blocked_solve(inverses, panels, all_features.T, block)
    gram = jnp.dot(all_features, prior_solved_t, precision=lax.Precision.HIGHEST)
    small = gram + train_count * jnp.eye(train_count, dtype=jnp.float32)
    small_inverse = inverse_factor(small)
    solved_all = train_count * mm(small_inverse.T, mm(small_inverse, prior_solved_t.T))
    solved_all = solved_all.astype(jnp.bfloat16)
    row_start = lax.axis_index("ex") * local_count
    solved = lax.dynamic_slice_in_dim(solved_all, row_start, local_count, 0)
    inverse_root = 1.0 / math.sqrt(feat_dim)
    block_probes = gather_rows(probes.astype(jnp.float32), "ex")
    return mm(block_probes, solved.astype(jnp.float32).T) * inverse_root


def solution(mesh):
    return jax.shard_map(
        per_device,
        mesh=mesh,
        in_specs=(
            P("ex", None, "param"),
            P("ex", None, "param"),
            P("param", None),
            P("param", None),
            P("ex", "param"),
            P(("param", "ex"), None),
        ),
        out_specs=P("param", "ex"),
        check_vma=False,
    )
```

```python
import math

import jax
import jax.numpy as jnp
from jax import lax
from jax.experimental import pallas as pl
from jax.experimental.pallas import tpu as pltpu
from jax.sharding import PartitionSpec as P


def _pick(row, index):
    lane = lax.broadcasted_iota(jnp.int32, row.shape, 1)
    return jnp.sum(jnp.where(lane == index, row, 0.0), axis=1, keepdims=True)


def _inverse_factor_kernel(a_ref, w_ref, s_ref):
    n = a_ref.shape[0]
    s_ref[...] = a_ref[...]
    rows = lax.broadcasted_iota(jnp.int32, (n, n), 0)
    cols = lax.broadcasted_iota(jnp.int32, (n, n), 1)
    w_ref[...] = jnp.where(rows == cols, 1.0, 0.0).astype(jnp.float32)
    for group in range(n // 8):
        low = group * 8

        def step(t, carry):
            j = low + 2 * t
            first = s_ref[pl.ds(j, 1), :]
            second = s_ref[pl.ds(j + 1, 1), :]
            first_inv = w_ref[pl.ds(j, 1), :]
            second_inv = w_ref[pl.ds(j + 1, 1), :]
            lead = _pick(first, j)
            cross = _pick(first, j + 1)
            tail = _pick(second, j + 1)
            scale0 = 1.0 / jnp.sqrt(lead)
            ratio = cross / lead
            scale1 = 1.0 / jnp.sqrt(tail - cross * ratio)
            second = (second - ratio * first) * scale1
            second_inv = (second_inv - ratio * first_inv) * scale1
            first = first * scale0
            first_inv = first_inv * scale0
            rest = s_ref[low:, :]
            lanes = lax.broadcasted_iota(jnp.int32, rest.shape, 1)
            col0 = jnp.sum(jnp.where(lanes == j, rest, 0.0), axis=1, keepdims=True)
            col1 = jnp.sum(jnp.where(lanes == j + 1, rest, 0.0), axis=1, keepdims=True)
            below = lax.broadcasted_iota(jnp.int32, (n - low, 1), 0) + low
            keep = below > j + 1
            factor0 = jnp.where(keep, col0 * scale0, 0.0)
            factor1 = jnp.where(keep, (col1 - col0 * ratio) * scale1, 0.0)
            s_ref[low:, :] = rest - factor0 * first - factor1 * second
            w_ref[low:, :] = w_ref[low:, :] - factor0 * first_inv - factor1 * second_inv
            s_ref[pl.ds(j, 1), :] = first
            s_ref[pl.ds(j + 1, 1), :] = second
            w_ref[pl.ds(j, 1), :] = first_inv
            w_ref[pl.ds(j + 1, 1), :] = second_inv
            return carry

        lax.fori_loop(0, 4, step, 0)


def inverse_factor(block):
    n = block.shape[0]
    return pl.pallas_call(
        _inverse_factor_kernel,
        out_shape=jax.ShapeDtypeStruct((n, n), jnp.float32),
        in_specs=[pl.BlockSpec(memory_space=pltpu.VMEM)],
        out_specs=pl.BlockSpec(memory_space=pltpu.VMEM),
        scratch_shapes=[pltpu.VMEM((n, n), jnp.float32)],
    )(block)


def outer_terms(factors, in_width):
    first = factors[:, :in_width]
    second = factors[:, in_width:]
    product = jnp.einsum("eol,eil->eoi", second, first, precision=lax.Precision.HIGHEST)
    return product.reshape(product.shape[0], -1)


def spd_solve(matrix, rhs_t):
    lower_factor = jnp.linalg.cholesky(matrix)
    halfway = lax.linalg.triangular_solve(lower_factor, rhs_t, left_side=True, lower=True)
    return lax.linalg.triangular_solve(
        lower_factor, halfway, left_side=True, lower=True, transpose_a=True
    )


def mm(a, b):
    return jnp.dot(a, b, precision=lax.Precision.HIGHEST, preferred_element_type=jnp.float32)


def blocked_cholesky(matrix, block):
    count = matrix.shape[0] // block
    inverses, panels = [], []
    trailing = matrix
    for k in range(count):
        inverse = inverse_factor(trailing[:block, :block])
        inverses.append(inverse)
        if k + 1 < count:
            panel = mm(trailing[block:, :block], inverse.T)
            panels.append(panel)
            trailing = trailing[block:, block:] - mm(panel, panel.T)
    return inverses, panels


def blocked_solve(inverses, panels, rhs, block):
    count = len(inverses)
    parts = []
    rest = rhs
    for k in range(count):
        part = mm(inverses[k], rest[:block])
        parts.append(part)
        if k + 1 < count:
            rest = rest[block:] - mm(panels[k], part)
    done = None
    for k in reversed(range(count)):
        target = parts[k]
        if done is not None:
            target = target - mm(panels[k].T, done)
        part = mm(inverses[k].T, target)
        done = part if done is None else jnp.concatenate((part, done), axis=0)
    return done


def gather_rows(block_rows, axis_name):
    count = lax.axis_size(axis_name)
    rows = block_rows.shape[0]
    padded = jnp.zeros((count * rows,) + block_rows.shape[1:], block_rows.dtype)
    padded = lax.dynamic_update_slice_in_dim(padded, block_rows, lax.axis_index(axis_name) * rows, 0)
    return lax.psum(padded, axis_name)


def gather_prior(prior):
    n_ex = lax.axis_size("ex")
    n_par = lax.axis_size("param")
    rows, cols = prior.shape
    blocks = lax.all_gather(prior, ("ex", "param"), axis=0, tiled=False)
    blocks = blocks.reshape(n_ex, n_par, rows, cols).transpose(0, 2, 1, 3)
    return blocks.reshape(n_ex * rows, n_par * cols)


def per_device(activations, out_grads, proj_in, proj_out, prior, probes):
    full_prior = gather_prior(prior)
    tokens = activations.shape[1]
    in_width = proj_in.shape[1]
    factor_in = jnp.einsum("eld,dk->ekl", activations, proj_in, preferred_element_type=jnp.float32)
    factor_out = jnp.einsum("eld,dk->ekl", out_grads, proj_out, preferred_element_type=jnp.float32)
    factors = jnp.concatenate((factor_in, factor_out), axis=1)
    factors = lax.psum(factors, "param")
    summed = outer_terms(factors, in_width)
    features = (summed * (1.0 / math.sqrt(tokens))).astype(jnp.bfloat16)
    local_count, feat_dim = features.shape
    all_features = gather_rows(features.astype(jnp.float32), "ex")
    train_count = all_features.shape[0]
    block = 128 if feat_dim % 128 == 0 else feat_dim
    inverses, panels = blocked_cholesky(full_prior, block)
    prior_solved_t = blocked_solve(inverses, panels, all_features.T, block)
    gram = jnp.dot(all_features, prior_solved_t, precision=lax.Precision.HIGHEST)
    small = gram + train_count * jnp.eye(train_count, dtype=jnp.float32)
    small_inverse = inverse_factor(small)
    solved_all = train_count * mm(small_inverse.T, mm(small_inverse, prior_solved_t.T))
    solved_all = solved_all.astype(jnp.bfloat16)
    row_start = lax.axis_index("ex") * local_count
    solved = lax.dynamic_slice_in_dim(solved_all, row_start, local_count, 0)
    inverse_root = 1.0 / math.sqrt(feat_dim)
    block_probes = gather_rows(probes.astype(jnp.float32), "ex")
    return mm(block_probes, solved.astype(jnp.float32).T) * inverse_root


def solution(mesh):
    return jax.shard_map(
        per_device,
        mesh=mesh,
        in_specs=(
            P("ex", None, "param"),
            P("ex", None, "param"),
            P("param", None),
            P("param", None),
            P("ex", "param"),
            P(("param", "ex"), None),
        ),
        out_specs=P("param", "ex"),
        check_vma=False,
    )
```

```python
import functools
import math

import jax
import jax.numpy as jnp
from jax import lax
from jax.experimental import pallas as pl
from jax.experimental.pallas import tpu as pltpu
from jax.sharding import PartitionSpec as P


def _pick(row, index):
    lane = lax.broadcasted_iota(jnp.int32, row.shape, 1)
    return jnp.sum(jnp.where(lane == index, row, 0.0), axis=1, keepdims=True)


def _inverse_factor_kernel(width, a_ref, w_ref, s_ref):
    n = a_ref.shape[0]
    s_ref[...] = a_ref[...]
    rows = lax.broadcasted_iota(jnp.int32, (n, n), 0)
    cols = lax.broadcasted_iota(jnp.int32, (n, n), 1)
    w_ref[...] = jnp.where(rows == cols, 1.0, 0.0).astype(jnp.float32)
    segment = 32 if n % 32 == 0 else 8
    for group in range(n // segment):
        low = group * segment

        def step(t, carry):
            j = low + width * t
            pivots = [s_ref[pl.ds(j + m, 1), :] for m in range(width)]
            inverses = [w_ref[pl.ds(j + m, 1), :] for m in range(width)]
            block = [[None] * width for _ in range(width)]
            for m in range(width):
                for l in range(m + 1):
                    block[m][l] = _pick(pivots[m], j + l)
                    block[l][m] = block[m][l]
            coeffs = [[1.0 if l == m else 0.0 for l in range(width)] for m in range(width)]
            for m in range(width):
                scale = 1.0 / jnp.sqrt(block[m][m])
                block[m] = [b * scale for b in block[m]]
                coeffs[m] = [c * scale for c in coeffs[m]]
                for q in range(m + 1, width):
                    factor = block[q][m] * scale
                    block[q] = [bq - factor * bm for bq, bm in zip(block[q], block[m])]
                    coeffs[q] = [cq - factor * cm for cq, cm in zip(coeffs[q], coeffs[m])]
            new_pivots, new_inverses = [], []
            for m in range(width):
                p = pivots[0] * coeffs[m][0]
                v = inverses[0] * coeffs[m][0]
                for l in range(1, m + 1):
                    p = p + pivots[l] * coeffs[m][l]
                    v = v + inverses[l] * coeffs[m][l]
                new_pivots.append(p)
                new_inverses.append(v)
            rest = s_ref[low:, :]
            lanes = lax.broadcasted_iota(jnp.int32, rest.shape, 1)
            columns = [jnp.sum(jnp.where(lanes == j + l, rest, 0.0), axis=1, keepdims=True) for l in range(width)]
            below = lax.broadcasted_iota(jnp.int32, (n - low, 1), 0) + low
            keep = below >= j + width
            new_rest = rest
            new_inv = w_ref[low:, :]
            for m in range(width):
                f = columns[0] * coeffs[m][0]
                for l in range(1, m + 1):
                    f = f + columns[l] * coeffs[m][l]
                f = jnp.where(keep, f, 0.0)
                new_rest = new_rest - f * new_pivots[m]
                new_inv = new_inv - f * new_inverses[m]
            s_ref[low:, :] = new_rest
            w_ref[low:, :] = new_inv
            for m in range(width):
                s_ref[pl.ds(j + m, 1), :] = new_pivots[m]
                w_ref[pl.ds(j + m, 1), :] = new_inverses[m]
            return carry

        lax.fori_loop(0, segment // width, step, 0)


def inverse_factor(block, width=4):
    n = block.shape[0]
    return pl.pallas_call(
        functools.partial(_inverse_factor_kernel, width),
        out_shape=jax.ShapeDtypeStruct((n, n), jnp.float32),
        in_specs=[pl.BlockSpec(memory_space=pltpu.VMEM)],
        out_specs=pl.BlockSpec(memory_space=pltpu.VMEM),
        scratch_shapes=[pltpu.VMEM((n, n), jnp.float32)],
    )(block)


def outer_terms(factors, in_width):
    first = factors[:, :in_width]
    second = factors[:, in_width:]
    product = jnp.einsum("eol,eil->eoi", second, first, precision=lax.Precision.HIGHEST)
    return product.reshape(product.shape[0], -1)


def spd_solve(matrix, rhs_t):
    lower_factor = jnp.linalg.cholesky(matrix)
    halfway = lax.linalg.triangular_solve(lower_factor, rhs_t, left_side=True, lower=True)
    return lax.linalg.triangular_solve(
        lower_factor, halfway, left_side=True, lower=True, transpose_a=True
    )


def mm(a, b):
    return jnp.dot(a, b, precision=lax.Precision.HIGHEST, preferred_element_type=jnp.float32)


def blocked_cholesky(matrix, block):
    count = matrix.shape[0] // block
    inverses, panels = [], []
    trailing = matrix
    for k in range(count):
        inverse = inverse_factor(trailing[:block, :block])
        inverses.append(inverse)
        if k + 1 < count:
            panel = mm(trailing[block:, :block], inverse.T)
            panels.append(panel)
            trailing = trailing[block:, block:] - mm(panel, panel.T)
    return inverses, panels


def blocked_solve(inverses, panels, rhs, block):
    count = len(inverses)
    parts = []
    rest = rhs
    for k in range(count):
        part = mm(inverses[k], rest[:block])
        parts.append(part)
        if k + 1 < count:
            rest = rest[block:] - mm(panels[k], part)
    done = None
    for k in reversed(range(count)):
        target = parts[k]
        if done is not None:
            target = target - mm(panels[k].T, done)
        part = mm(inverses[k].T, target)
        done = part if done is None else jnp.concatenate((part, done), axis=0)
    return done


def gather_rows(block_rows, axis_name):
    count = lax.axis_size(axis_name)
    rows = block_rows.shape[0]
    padded = jnp.zeros((count * rows,) + block_rows.shape[1:], block_rows.dtype)
    padded = lax.dynamic_update_slice_in_dim(padded, block_rows, lax.axis_index(axis_name) * rows, 0)
    return lax.psum(padded, axis_name)


def gather_prior(prior):
    n_ex = lax.axis_size("ex")
    n_par = lax.axis_size("param")
    rows, cols = prior.shape
    blocks = lax.all_gather(prior, ("ex", "param"), axis=0, tiled=False)
    blocks = blocks.reshape(n_ex, n_par, rows, cols).transpose(0, 2, 1, 3)
    return blocks.reshape(n_ex * rows, n_par * cols)


def per_device(activations, out_grads, proj_in, proj_out, prior, probes):
    full_prior = gather_prior(prior)
    tokens = activations.shape[1]
    in_width = proj_in.shape[1]
    factor_in = jnp.einsum("eld,dk->ekl", activations, proj_in, preferred_element_type=jnp.float32)
    factor_out = jnp.einsum("eld,dk->ekl", out_grads, proj_out, preferred_element_type=jnp.float32)
    factors = jnp.concatenate((factor_in, factor_out), axis=1)
    factors = lax.psum(factors, "param")
    summed = outer_terms(factors, in_width)
    features = (summed * (1.0 / math.sqrt(tokens))).astype(jnp.bfloat16)
    local_count, feat_dim = features.shape
    all_features = gather_rows(features.astype(jnp.float32), "ex")
    train_count = all_features.shape[0]
    block = 128 if feat_dim % 128 == 0 else feat_dim
    inverses, panels = blocked_cholesky(full_prior, block)
    prior_solved_t = blocked_solve(inverses, panels, all_features.T, block)
    gram = jnp.dot(all_features, prior_solved_t, precision=lax.Precision.HIGHEST)
    small = gram + train_count * jnp.eye(train_count, dtype=jnp.float32)
    small_inverse = inverse_factor(small)
    solved_all = train_count * mm(small_inverse.T, mm(small_inverse, prior_solved_t.T))
    solved_all = solved_all.astype(jnp.bfloat16)
    row_start = lax.axis_index("ex") * local_count
    solved = lax.dynamic_slice_in_dim(solved_all, row_start, local_count, 0)
    inverse_root = 1.0 / math.sqrt(feat_dim)
    block_probes = gather_rows(probes.astype(jnp.float32), "ex")
    return mm(block_probes, solved.astype(jnp.float32).T) * inverse_root


def solution(mesh):
    return jax.shard_map(
        per_device,
        mesh=mesh,
        in_specs=(
            P("ex", None, "param"),
            P("ex", None, "param"),
            P("param", None),
            P("param", None),
            P("ex", "param"),
            P(("param", "ex"), None),
        ),
        out_specs=P("param", "ex"),
        check_vma=False,
    )
```

```python
import functools
import math

import jax
import jax.numpy as jnp
from jax import lax
from jax.experimental import pallas as pl
from jax.experimental.pallas import tpu as pltpu
from jax.sharding import PartitionSpec as P


def _pick(row, index):
    lane = lax.broadcasted_iota(jnp.int32, row.shape, 1)
    return jnp.sum(jnp.where(lane == index, row, 0.0), axis=1, keepdims=True)


def _inverse_factor_kernel(width, a_ref, w_ref, s_ref):
    n = a_ref.shape[0]
    s_ref[...] = a_ref[...]
    rows = lax.broadcasted_iota(jnp.int32, (n, n), 0)
    cols = lax.broadcasted_iota(jnp.int32, (n, n), 1)
    w_ref[...] = jnp.where(rows == cols, 1.0, 0.0).astype(jnp.float32)
    segment = 32 if n % 32 == 0 else 8
    for group in range(n // segment):
        low = group * segment

        def step(t, carry):
            j = low + width * t
            pivots = [s_ref[pl.ds(j + m, 1), :] for m in range(width)]
            inverses = [w_ref[pl.ds(j + m, 1), :] for m in range(width)]
            block = [[None] * width for _ in range(width)]
            for m in range(width):
                for l in range(m + 1):
                    block[m][l] = _pick(pivots[m], j + l)
                    block[l][m] = block[m][l]
            coeffs = [[1.0 if l == m else 0.0 for l in range(width)] for m in range(width)]
            for m in range(width):
                scale = 1.0 / jnp.sqrt(block[m][m])
                block[m] = [b * scale for b in block[m]]
                coeffs[m] = [c * scale for c in coeffs[m]]
                for q in range(m + 1, width):
                    factor = block[q][m] * scale
                    block[q] = [bq - factor * bm for bq, bm in zip(block[q], block[m])]
                    coeffs[q] = [cq - factor * cm for cq, cm in zip(coeffs[q], coeffs[m])]
            new_pivots, new_inverses = [], []
            for m in range(width):
                p = pivots[0] * coeffs[m][0]
                v = inverses[0] * coeffs[m][0]
                for l in range(1, m + 1):
                    p = p + pivots[l] * coeffs[m][l]
                    v = v + inverses[l] * coeffs[m][l]
                new_pivots.append(p)
                new_inverses.append(v)
            rest = s_ref[low:, :]
            lanes = lax.broadcasted_iota(jnp.int32, rest.shape, 1)
            columns = [jnp.sum(jnp.where(lanes == j + l, rest, 0.0), axis=1, keepdims=True) for l in range(width)]
            below = lax.broadcasted_iota(jnp.int32, (n - low, 1), 0) + low
            keep = below >= j + width
            new_rest = rest
            new_inv = w_ref[low:, :]
            for m in range(width):
                f = columns[0] * coeffs[m][0]
                for l in range(1, m + 1):
                    f = f + columns[l] * coeffs[m][l]
                f = jnp.where(keep, f, 0.0)
                new_rest = new_rest - f * new_pivots[m]
                new_inv = new_inv - f * new_inverses[m]
            s_ref[low:, :] = new_rest
            w_ref[low:, :] = new_inv
            for m in range(width):
                s_ref[pl.ds(j + m, 1), :] = new_pivots[m]
                w_ref[pl.ds(j + m, 1), :] = new_inverses[m]
            return carry

        lax.fori_loop(0, segment // width, step, 0)


def inverse_factor(block, width=4):
    n = block.shape[0]
    return pl.pallas_call(
        functools.partial(_inverse_factor_kernel, width),
        out_shape=jax.ShapeDtypeStruct((n, n), jnp.float32),
        in_specs=[pl.BlockSpec(memory_space=pltpu.VMEM)],
        out_specs=pl.BlockSpec(memory_space=pltpu.VMEM),
        scratch_shapes=[pltpu.VMEM((n, n), jnp.float32)],
    )(block)


def outer_terms(factors, in_width):
    first = factors[:, :in_width]
    second = factors[:, in_width:]
    product = jnp.einsum("eol,eil->eoi", second, first, precision=lax.Precision.HIGHEST)
    return product.reshape(product.shape[0], -1)


def spd_solve(matrix, rhs_t):
    lower_factor = jnp.linalg.cholesky(matrix)
    halfway = lax.linalg.triangular_solve(lower_factor, rhs_t, left_side=True, lower=True)
    return lax.linalg.triangular_solve(
        lower_factor, halfway, left_side=True, lower=True, transpose_a=True
    )


def mm(a, b):
    return jnp.dot(a, b, precision=lax.Precision.HIGHEST, preferred_element_type=jnp.float32)


def block_eliminate(matrix, rhs, block):
    count = matrix.shape[0] // block
    trailing = jnp.concatenate((matrix, rhs), axis=1)
    tops = []
    for k in range(count):
        inverse = inverse_factor(trailing[:block, :block])
        top = mm(inverse.T, mm(inverse, trailing[:block, block:]))
        tops.append(top)
        if k + 1 < count:
            trailing = trailing[block:, block:] - mm(trailing[block:, :block], top)
    done = tops[-1]
    for k in reversed(range(count - 1)):
        width = done.shape[0]
        part = tops[k][:, width:] - mm(tops[k][:, :width], done)
        done = jnp.concatenate((part, done), axis=0)
    return done


def gather_rows(block_rows, axis_name):
    count = lax.axis_size(axis_name)
    rows = block_rows.shape[0]
    padded = jnp.zeros((count * rows,) + block_rows.shape[1:], block_rows.dtype)
    padded = lax.dynamic_update_slice_in_dim(padded, block_rows, lax.axis_index(axis_name) * rows, 0)
    return lax.psum(padded, axis_name)


def gather_prior(prior):
    n_ex = lax.axis_size("ex")
    n_par = lax.axis_size("param")
    rows, cols = prior.shape
    blocks = lax.all_gather(prior, ("ex", "param"), axis=0, tiled=False)
    blocks = blocks.reshape(n_ex, n_par, rows, cols).transpose(0, 2, 1, 3)
    return blocks.reshape(n_ex * rows, n_par * cols)


def per_device(activations, out_grads, proj_in, proj_out, prior, probes):
    full_prior = gather_prior(prior)
    tokens = activations.shape[1]
    in_width = proj_in.shape[1]
    factor_in = jnp.einsum("eld,dk->ekl", activations, proj_in, preferred_element_type=jnp.float32)
    factor_out = jnp.einsum("eld,dk->ekl", out_grads, proj_out, preferred_element_type=jnp.float32)
    factors = jnp.concatenate((factor_in, factor_out), axis=1)
    factors = lax.psum(factors, "param")
    summed = outer_terms(factors, in_width)
    features = (summed * (1.0 / math.sqrt(tokens))).astype(jnp.bfloat16)
    local_count, feat_dim = features.shape
    all_features = gather_rows(features.astype(jnp.float32), "ex")
    train_count = all_features.shape[0]
    block = 128 if feat_dim % 128 == 0 else feat_dim
    prior_solved_t = block_eliminate(full_prior, all_features.T, block)
    gram = jnp.dot(all_features, prior_solved_t, precision=lax.Precision.HIGHEST)
    small = gram + train_count * jnp.eye(train_count, dtype=jnp.float32)
    small_inverse = inverse_factor(small)
    solved_all = train_count * mm(small_inverse.T, mm(small_inverse, prior_solved_t.T))
    solved_all = solved_all.astype(jnp.bfloat16)
    row_start = lax.axis_index("ex") * local_count
    solved = lax.dynamic_slice_in_dim(solved_all, row_start, local_count, 0)
    inverse_root = 1.0 / math.sqrt(feat_dim)
    block_probes = gather_rows(probes.astype(jnp.float32) + 0.0 * all_features[:1, :1], "ex")
    return mm(block_probes, solved.astype(jnp.float32).T) * inverse_root


def solution(mesh):
    return jax.shard_map(
        per_device,
        mesh=mesh,
        in_specs=(
            P("ex", None, "param"),
            P("ex", None, "param"),
            P("param", None),
            P("param", None),
            P("ex", "param"),
            P(("param", "ex"), None),
        ),
        out_specs=P("param", "ex"),
        check_vma=False,
    )
```

```python
import functools
import math

import jax
import jax.numpy as jnp
from jax import lax
from jax.experimental import pallas as pl
from jax.experimental.pallas import tpu as pltpu
from jax.sharding import PartitionSpec as P


def _pick(row, index):
    lane = lax.broadcasted_iota(jnp.int32, row.shape, 1)
    return jnp.sum(jnp.where(lane == index, row, 0.0), axis=1, keepdims=True)


def _inverse_factor_kernel(width, a_ref, w_ref, s_ref):
    n = a_ref.shape[0]
    s_ref[...] = a_ref[...]
    rows = lax.broadcasted_iota(jnp.int32, (n, n), 0)
    cols = lax.broadcasted_iota(jnp.int32, (n, n), 1)
    w_ref[...] = jnp.where(rows == cols, 1.0, 0.0).astype(jnp.float32)
    segment = 32 if n % 32 == 0 else 8
    for group in range(n // segment):
        low = group * segment

        def step(t, carry):
            j = low + width * t
            pivots = [s_ref[pl.ds(j + m, 1), :] for m in range(width)]
            inverses = [w_ref[pl.ds(j + m, 1), :] for m in range(width)]
            block = [[None] * width for _ in range(width)]
            for m in range(width):
                for l in range(m + 1):
                    block[m][l] = _pick(pivots[m], j + l)
                    block[l][m] = block[m][l]
            coeffs = [[1.0 if l == m else 0.0 for l in range(width)] for m in range(width)]
            for m in range(width):
                scale = 1.0 / jnp.sqrt(block[m][m])
                block[m] = [b * scale for b in block[m]]
                coeffs[m] = [c * scale for c in coeffs[m]]
                for q in range(m + 1, width):
                    factor = block[q][m] * scale
                    block[q] = [bq - factor * bm for bq, bm in zip(block[q], block[m])]
                    coeffs[q] = [cq - factor * cm for cq, cm in zip(coeffs[q], coeffs[m])]
            new_pivots, new_inverses = [], []
            for m in range(width):
                p = pivots[0] * coeffs[m][0]
                v = inverses[0] * coeffs[m][0]
                for l in range(1, m + 1):
                    p = p + pivots[l] * coeffs[m][l]
                    v = v + inverses[l] * coeffs[m][l]
                new_pivots.append(p)
                new_inverses.append(v)
            rest = s_ref[low:, :]
            lanes = lax.broadcasted_iota(jnp.int32, rest.shape, 1)
            columns = [jnp.sum(jnp.where(lanes == j + l, rest, 0.0), axis=1, keepdims=True) for l in range(width)]
            below = lax.broadcasted_iota(jnp.int32, (n - low, 1), 0) + low
            keep = below >= j + width
            new_rest = rest
            new_inv = w_ref[low:, :]
            for m in range(width):
                f = columns[0] * coeffs[m][0]
                for l in range(1, m + 1):
                    f = f + columns[l] * coeffs[m][l]
                f = jnp.where(keep, f, 0.0)
                new_rest = new_rest - f * new_pivots[m]
                new_inv = new_inv - f * new_inverses[m]
            s_ref[low:, :] = new_rest
            w_ref[low:, :] = new_inv
            for m in range(width):
                s_ref[pl.ds(j + m, 1), :] = new_pivots[m]
                w_ref[pl.ds(j + m, 1), :] = new_inverses[m]
            return carry

        lax.fori_loop(0, segment // width, step, 0)


def inverse_factor(block, width=4):
    n = block.shape[0]
    return pl.pallas_call(
        functools.partial(_inverse_factor_kernel, width),
        out_shape=jax.ShapeDtypeStruct((n, n), jnp.float32),
        in_specs=[pl.BlockSpec(memory_space=pltpu.VMEM)],
        out_specs=pl.BlockSpec(memory_space=pltpu.VMEM),
        scratch_shapes=[pltpu.VMEM((n, n), jnp.float32)],
    )(block)


def outer_terms(factors, in_width):
    first = factors[:, :in_width]
    second = factors[:, in_width:]
    product = jnp.einsum("eol,eil->eoi", second, first, precision=lax.Precision.HIGHEST)
    return product.reshape(product.shape[0], -1)


def spd_solve(matrix, rhs_t):
    lower_factor = jnp.linalg.cholesky(matrix)
    halfway = lax.linalg.triangular_solve(lower_factor, rhs_t, left_side=True, lower=True)
    return lax.linalg.triangular_solve(
        lower_factor, halfway, left_side=True, lower=True, transpose_a=True
    )


def mm(a, b):
    return jnp.dot(a, b, precision=lax.Precision.HIGHEST, preferred_element_type=jnp.float32)


def blocked_cholesky(matrix, block):
    count = matrix.shape[0] // block
    inverses, panels = [], []
    trailing = matrix
    for k in range(count):
        inverse = inverse_factor(trailing[:block, :block])
        inverses.append(inverse)
        if k + 1 < count:
            panel = mm(trailing[block:, :block], inverse.T)
            panels.append(panel)
            trailing = trailing[block:, block:] - mm(panel, panel.T)
    return inverses, panels


def blocked_solve(inverses, panels, rhs, block):
    count = len(inverses)
    parts = []
    rest = rhs
    for k in range(count):
        part = mm(inverses[k], rest[:block])
        parts.append(part)
        if k + 1 < count:
            rest = rest[block:] - mm(panels[k], part)
    done = None
    for k in reversed(range(count)):
        target = parts[k]
        if done is not None:
            target = target - mm(panels[k].T, done)
        part = mm(inverses[k].T, target)
        done = part if done is None else jnp.concatenate((part, done), axis=0)
    return done


def gather_rows(block_rows, axis_name):
    count = lax.axis_size(axis_name)
    rows = block_rows.shape[0]
    padded = jnp.zeros((count * rows,) + block_rows.shape[1:], block_rows.dtype)
    padded = lax.dynamic_update_slice_in_dim(padded, block_rows, lax.axis_index(axis_name) * rows, 0)
    return lax.psum(padded, axis_name)


def gather_prior(prior):
    n_ex = lax.axis_size("ex")
    n_par = lax.axis_size("param")
    rows, cols = prior.shape
    blocks = lax.all_gather(prior, ("ex", "param"), axis=0, tiled=False)
    return jnp.concatenate(
        [jnp.concatenate([blocks[e * n_par + p] for p in range(n_par)], axis=1) for e in range(n_ex)], axis=0
    )


def per_device(activations, out_grads, proj_in, proj_out, prior, probes):
    full_prior = gather_prior(prior)
    tokens = activations.shape[1]
    in_width = proj_in.shape[1]
    factor_in = jnp.einsum("eld,dk->ekl", activations, proj_in, preferred_element_type=jnp.float32)
    factor_out = jnp.einsum("eld,dk->ekl", out_grads, proj_out, preferred_element_type=jnp.float32)
    factors = jnp.concatenate((factor_in, factor_out), axis=1)
    factors = lax.psum(factors, "param")
    summed = outer_terms(factors, in_width)
    features = (summed * (1.0 / math.sqrt(tokens))).astype(jnp.bfloat16)
    local_count, feat_dim = features.shape
    all_features = gather_rows(features.astype(jnp.float32), "ex")
    train_count = all_features.shape[0]
    block = 128 if feat_dim % 128 == 0 else feat_dim
    inverses, panels = blocked_cholesky(full_prior, block)
    prior_solved_t = blocked_solve(inverses, panels, all_features.T, block)
    gram = jnp.dot(all_features, prior_solved_t, precision=lax.Precision.HIGHEST)
    small = gram + train_count * jnp.eye(train_count, dtype=jnp.float32)
    small_inverse = inverse_factor(small)
    solved_all = train_count * mm(small_inverse.T, mm(small_inverse, prior_solved_t.T))
    solved_all = solved_all.astype(jnp.bfloat16)
    row_start = lax.axis_index("ex") * local_count
    solved = lax.dynamic_slice_in_dim(solved_all, row_start, local_count, 0)
    inverse_root = 1.0 / math.sqrt(feat_dim)
    block_probes = gather_rows(probes.astype(jnp.float32), "ex")
    return mm(block_probes, solved.astype(jnp.float32).T) * inverse_root


def solution(mesh):
    return jax.shard_map(
        per_device,
        mesh=mesh,
        in_specs=(
            P("ex", None, "param"),
            P("ex", None, "param"),
            P("param", None),
            P("param", None),
            P("ex", "param"),
            P(("param", "ex"), None),
        ),
        out_specs=P("param", "ex"),
        check_vma=False,
    )
```

```python
import functools
import math

import jax
import jax.numpy as jnp
from jax import lax
from jax.experimental import pallas as pl
from jax.experimental.pallas import tpu as pltpu
from jax.sharding import PartitionSpec as P


def _pick(row, index):
    lane = lax.broadcasted_iota(jnp.int32, row.shape, 1)
    return jnp.sum(jnp.where(lane == index, row, 0.0), axis=1, keepdims=True)


def _inverse_factor_kernel(width, a_ref, w_ref, s_ref):
    n = a_ref.shape[0]
    s_ref[...] = a_ref[...]
    rows = lax.broadcasted_iota(jnp.int32, (n, n), 0)
    cols = lax.broadcasted_iota(jnp.int32, (n, n), 1)
    w_ref[...] = jnp.where(rows == cols, 1.0, 0.0).astype(jnp.float32)
    segment = 32 if n % 32 == 0 else 8
    for group in range(n // segment):
        low = group * segment

        def step(t, carry):
            j = low + width * t
            pivots = [s_ref[pl.ds(j + m, 1), :] for m in range(width)]
            inverses = [w_ref[pl.ds(j + m, 1), :] for m in range(width)]
            block = [[None] * width for _ in range(width)]
            for m in range(width):
                for l in range(m + 1):
                    block[m][l] = _pick(pivots[m], j + l)
                    block[l][m] = block[m][l]
            coeffs = [[1.0 if l == m else 0.0 for l in range(width)] for m in range(width)]
            for m in range(width):
                scale = 1.0 / jnp.sqrt(block[m][m])
                block[m] = [b * scale for b in block[m]]
                coeffs[m] = [c * scale for c in coeffs[m]]
                for q in range(m + 1, width):
                    factor = block[q][m] * scale
                    block[q] = [bq - factor * bm for bq, bm in zip(block[q], block[m])]
                    coeffs[q] = [cq - factor * cm for cq, cm in zip(coeffs[q], coeffs[m])]
            new_pivots, new_inverses = [], []
            for m in range(width):
                p = pivots[0] * coeffs[m][0]
                v = inverses[0] * coeffs[m][0]
                for l in range(1, m + 1):
                    p = p + pivots[l] * coeffs[m][l]
                    v = v + inverses[l] * coeffs[m][l]
                new_pivots.append(p)
                new_inverses.append(v)
            rest = s_ref[low:, :]
            lanes = lax.broadcasted_iota(jnp.int32, rest.shape, 1)
            columns = [jnp.sum(jnp.where(lanes == j + l, rest, 0.0), axis=1, keepdims=True) for l in range(width)]
            below = lax.broadcasted_iota(jnp.int32, (n - low, 1), 0) + low
            keep = below >= j + width
            new_rest = rest
            new_inv = w_ref[low:, :]
            for m in range(width):
                f = columns[0] * coeffs[m][0]
                for l in range(1, m + 1):
                    f = f + columns[l] * coeffs[m][l]
                f = jnp.where(keep, f, 0.0)
                new_rest = new_rest - f * new_pivots[m]
                new_inv = new_inv - f * new_inverses[m]
            s_ref[low:, :] = new_rest
            w_ref[low:, :] = new_inv
            for m in range(width):
                s_ref[pl.ds(j + m, 1), :] = new_pivots[m]
                w_ref[pl.ds(j + m, 1), :] = new_inverses[m]
            return carry

        lax.fori_loop(0, segment // width, step, 0)


def inverse_factor(block, width=4):
    n = block.shape[0]
    return pl.pallas_call(
        functools.partial(_inverse_factor_kernel, width),
        out_shape=jax.ShapeDtypeStruct((n, n), jnp.float32),
        in_specs=[pl.BlockSpec(memory_space=pltpu.VMEM)],
        out_specs=pl.BlockSpec(memory_space=pltpu.VMEM),
        scratch_shapes=[pltpu.VMEM((n, n), jnp.float32)],
    )(block)


def outer_terms(factors, in_width):
    first = factors[:, :in_width]
    second = factors[:, in_width:]
    product = jnp.einsum("eol,eil->eoi", second, first, precision=lax.Precision.HIGHEST)
    return product.reshape(product.shape[0], -1)


def spd_solve(matrix, rhs_t):
    lower_factor = jnp.linalg.cholesky(matrix)
    halfway = lax.linalg.triangular_solve(lower_factor, rhs_t, left_side=True, lower=True)
    return lax.linalg.triangular_solve(
        lower_factor, halfway, left_side=True, lower=True, transpose_a=True
    )


def mm(a, b):
    return jnp.dot(a, b, precision=lax.Precision.HIGHEST, preferred_element_type=jnp.float32)


def blocked_cholesky(matrix, block):
    count = matrix.shape[0] // block
    inverses, panels = [], []
    trailing = matrix
    for k in range(count):
        inverse = inverse_factor(trailing[:block, :block])
        inverses.append(inverse)
        if k + 1 < count:
            panel = mm(trailing[block:, :block], inverse.T)
            panels.append(panel)
            trailing = trailing[block:, block:] - mm(panel, panel.T)
    return inverses, panels


def blocked_solve(inverses, panels, rhs, block):
    count = len(inverses)
    parts = []
    rest = rhs
    for k in range(count):
        part = mm(inverses[k], rest[:block])
        parts.append(part)
        if k + 1 < count:
            rest = rest[block:] - mm(panels[k], part)
    done = None
    for k in reversed(range(count)):
        target = parts[k]
        if done is not None:
            target = target - mm(panels[k].T, done)
        part = mm(inverses[k].T, target)
        done = part if done is None else jnp.concatenate((part, done), axis=0)
    return done


def gather_rows(block_rows, axis_name):
    count = lax.axis_size(axis_name)
    rows = block_rows.shape[0]
    padded = jnp.zeros((count * rows,) + block_rows.shape[1:], block_rows.dtype)
    padded = lax.dynamic_update_slice_in_dim(padded, block_rows, lax.axis_index(axis_name) * rows, 0)
    return lax.psum(padded, axis_name)


def gather_prior(prior):
    n_ex = lax.axis_size("ex")
    n_par = lax.axis_size("param")
    rows, cols = prior.shape
    blocks = lax.all_gather(prior, ("ex", "param"), axis=0, tiled=False)
    return jnp.concatenate(
        [jnp.concatenate([blocks[e * n_par + p] for p in range(n_par)], axis=1) for e in range(n_ex)], axis=0
    )


def per_device(activations, out_grads, proj_in, proj_out, prior, probes):
    full_prior = gather_prior(prior)
    tokens = activations.shape[1]
    in_width = proj_in.shape[1]
    factor_in = jnp.einsum("eld,dk->ekl", activations, proj_in, preferred_element_type=jnp.float32)
    factor_out = jnp.einsum("eld,dk->ekl", out_grads, proj_out, preferred_element_type=jnp.float32)
    factors = jnp.concatenate((factor_in, factor_out), axis=1)
    factors = lax.psum(factors, "param")
    summed = outer_terms(factors, in_width)
    features = (summed * (1.0 / math.sqrt(tokens))).astype(jnp.bfloat16)
    local_count, feat_dim = features.shape
    everyone = lax.all_gather(features.astype(jnp.float32), ("ex", "param"), axis=0, tiled=False)
    all_features = everyone.reshape(lax.axis_size("ex"), lax.axis_size("param"), local_count, feat_dim)[:, 0]
    all_features = all_features.reshape(-1, feat_dim)
    train_count = all_features.shape[0]
    block = 128 if feat_dim % 128 == 0 else feat_dim
    inverses, panels = blocked_cholesky(full_prior, block)
    prior_solved_t = blocked_solve(inverses, panels, all_features.T, block)
    gram = jnp.dot(all_features, prior_solved_t, precision=lax.Precision.HIGHEST)
    small = gram + train_count * jnp.eye(train_count, dtype=jnp.float32)
    small_inverse = inverse_factor(small)
    solved_all = train_count * mm(small_inverse.T, mm(small_inverse, prior_solved_t.T))
    solved_all = solved_all.astype(jnp.bfloat16)
    row_start = lax.axis_index("ex") * local_count
    solved = lax.dynamic_slice_in_dim(solved_all, row_start, local_count, 0)
    inverse_root = 1.0 / math.sqrt(feat_dim)
    block_probes = gather_rows(probes.astype(jnp.float32), "ex")
    return mm(block_probes, solved.astype(jnp.float32).T) * inverse_root


def solution(mesh):
    return jax.shard_map(
        per_device,
        mesh=mesh,
        in_specs=(
            P("ex", None, "param"),
            P("ex", None, "param"),
            P("param", None),
            P("param", None),
            P("ex", "param"),
            P(("param", "ex"), None),
        ),
        out_specs=P("param", "ex"),
        check_vma=False,
    )
```

```python
import functools
import math

import jax
import jax.numpy as jnp
from jax import lax
from jax.experimental import pallas as pl
from jax.experimental.pallas import tpu as pltpu
from jax.sharding import PartitionSpec as P


def _pick(row, index):
    lane = lax.broadcasted_iota(jnp.int32, row.shape, 1)
    return jnp.sum(jnp.where(lane == index, row, 0.0), axis=1, keepdims=True)


def _inverse_factor_kernel(width, a_ref, w_ref, s_ref):
    n = a_ref.shape[0]
    s_ref[...] = a_ref[...]
    rows = lax.broadcasted_iota(jnp.int32, (n, n), 0)
    cols = lax.broadcasted_iota(jnp.int32, (n, n), 1)
    w_ref[...] = jnp.where(rows == cols, 1.0, 0.0).astype(jnp.float32)
    segment = 32 if n % 32 == 0 else 8
    for group in range(n // segment):
        low = group * segment

        def step(t, carry):
            j = low + width * t
            pivots = [s_ref[pl.ds(j + m, 1), :] for m in range(width)]
            inverses = [w_ref[pl.ds(j + m, 1), :] for m in range(width)]
            block = [[None] * width for _ in range(width)]
            for m in range(width):
                for l in range(m + 1):
                    block[m][l] = _pick(pivots[m], j + l)
                    block[l][m] = block[m][l]
            coeffs = [[1.0 if l == m else 0.0 for l in range(width)] for m in range(width)]
            for m in range(width):
                scale = 1.0 / jnp.sqrt(block[m][m])
                block[m] = [b * scale for b in block[m]]
                coeffs[m] = [c * scale for c in coeffs[m]]
                for q in range(m + 1, width):
                    factor = block[q][m] * scale
                    block[q] = [bq - factor * bm for bq, bm in zip(block[q], block[m])]
                    coeffs[q] = [cq - factor * cm for cq, cm in zip(coeffs[q], coeffs[m])]
            new_pivots, new_inverses = [], []
            for m in range(width):
                p = pivots[0] * coeffs[m][0]
                v = inverses[0] * coeffs[m][0]
                for l in range(1, m + 1):
                    p = p + pivots[l] * coeffs[m][l]
                    v = v + inverses[l] * coeffs[m][l]
                new_pivots.append(p)
                new_inverses.append(v)
            rest = s_ref[low:, :]
            lanes = lax.broadcasted_iota(jnp.int32, rest.shape, 1)
            columns = [jnp.sum(jnp.where(lanes == j + l, rest, 0.0), axis=1, keepdims=True) for l in range(width)]
            below = lax.broadcasted_iota(jnp.int32, (n - low, 1), 0) + low
            keep = below >= j + width
            new_rest = rest
            new_inv = w_ref[low:, :]
            for m in range(width):
                f = columns[0] * coeffs[m][0]
                for l in range(1, m + 1):
                    f = f + columns[l] * coeffs[m][l]
                f = jnp.where(keep, f, 0.0)
                new_rest = new_rest - f * new_pivots[m]
                new_inv = new_inv - f * new_inverses[m]
            s_ref[low:, :] = new_rest
            w_ref[low:, :] = new_inv
            for m in range(width):
                s_ref[pl.ds(j + m, 1), :] = new_pivots[m]
                w_ref[pl.ds(j + m, 1), :] = new_inverses[m]
            return carry

        lax.fori_loop(0, segment // width, step, 0)


def inverse_factor(block, width=4):
    n = block.shape[0]
    return pl.pallas_call(
        functools.partial(_inverse_factor_kernel, width),
        out_shape=jax.ShapeDtypeStruct((n, n), jnp.float32),
        in_specs=[pl.BlockSpec(memory_space=pltpu.VMEM)],
        out_specs=pl.BlockSpec(memory_space=pltpu.VMEM),
        scratch_shapes=[pltpu.VMEM((n, n), jnp.float32)],
    )(block)


def outer_terms(factors, in_width):
    first = factors[:, :in_width]
    second = factors[:, in_width:]
    product = jnp.einsum("eol,eil->eoi", second, first, precision=lax.Precision.HIGHEST)
    return product.reshape(product.shape[0], -1)


def spd_solve(matrix, rhs_t):
    lower_factor = jnp.linalg.cholesky(matrix)
    halfway = lax.linalg.triangular_solve(lower_factor, rhs_t, left_side=True, lower=True)
    return lax.linalg.triangular_solve(
        lower_factor, halfway, left_side=True, lower=True, transpose_a=True
    )


def mm(a, b):
    return jnp.dot(a, b, precision=lax.Precision.HIGHEST, preferred_element_type=jnp.float32)


def blocked_cholesky(matrix, block):
    count = matrix.shape[0] // block
    inverses, panels = [], []
    trailing = matrix
    for k in range(count):
        inverse = inverse_factor(trailing[:block, :block])
        inverses.append(inverse)
        if k + 1 < count:
            panel = mm(trailing[block:, :block], inverse.T)
            panels.append(panel)
            trailing = trailing[block:, block:] - mm(panel, panel.T)
    return inverses, panels


def blocked_solve(inverses, panels, rhs, block):
    count = len(inverses)
    parts = []
    rest = rhs
    for k in range(count):
        part = mm(inverses[k], rest[:block])
        parts.append(part)
        if k + 1 < count:
            rest = rest[block:] - mm(panels[k], part)
    done = None
    for k in reversed(range(count)):
        target = parts[k]
        if done is not None:
            target = target - mm(panels[k].T, done)
        part = mm(inverses[k].T, target)
        done = part if done is None else jnp.concatenate((part, done), axis=0)
    return done


def gather_rows(block_rows, axis_name):
    count = lax.axis_size(axis_name)
    rows = block_rows.shape[0]
    padded = jnp.zeros((count * rows,) + block_rows.shape[1:], block_rows.dtype)
    padded = lax.dynamic_update_slice_in_dim(padded, block_rows, lax.axis_index(axis_name) * rows, 0)
    return lax.psum(padded, axis_name)


def gather_prior(prior):
    n_ex = lax.axis_size("ex")
    n_par = lax.axis_size("param")
    rows, cols = prior.shape
    blocks = lax.all_gather(prior, ("ex", "param"), axis=0, tiled=False)
    return jnp.concatenate(
        [jnp.concatenate([blocks[e * n_par + p] for p in range(n_par)], axis=1) for e in range(n_ex)], axis=0
    )


def per_device(activations, out_grads, proj_in, proj_out, prior, probes):
    full_prior = gather_prior(prior)
    tokens = activations.shape[1]
    in_width = proj_in.shape[1]
    factor_in = jnp.einsum("eld,dk->ekl", activations, proj_in, preferred_element_type=jnp.float32)
    factor_out = jnp.einsum("eld,dk->ekl", out_grads, proj_out, preferred_element_type=jnp.float32)
    factors = jnp.concatenate((factor_in, factor_out), axis=1)
    local_count = factors.shape[0]
    n_ex = lax.axis_size("ex")
    if n_ex * factors.size * 4 <= (2 << 20):
        padded = jnp.zeros((n_ex * local_count,) + factors.shape[1:], factors.dtype)
        padded = lax.dynamic_update_slice_in_dim(padded, factors, lax.axis_index("ex") * local_count, 0)
        all_factors = lax.psum(padded, ("ex", "param"))
        summed = outer_terms(all_factors, in_width)
        features = (summed * (1.0 / math.sqrt(tokens))).astype(jnp.bfloat16)
        feat_dim = features.shape[1]
        all_features = features.astype(jnp.float32)
    else:
        factors = lax.psum(factors, "param")
        summed = outer_terms(factors, in_width)
        features = (summed * (1.0 / math.sqrt(tokens))).astype(jnp.bfloat16)
        feat_dim = features.shape[1]
        everyone = lax.all_gather(features.astype(jnp.float32), ("ex", "param"), axis=0, tiled=False)
        all_features = everyone.reshape(n_ex, lax.axis_size("param"), local_count, feat_dim)[:, 0]
        all_features = all_features.reshape(-1, feat_dim)
    train_count = all_features.shape[0]
    block = 128 if feat_dim % 128 == 0 else feat_dim
    inverses, panels = blocked_cholesky(full_prior, block)
    prior_solved_t = blocked_solve(inverses, panels, all_features.T, block)
    gram = jnp.dot(all_features, prior_solved_t, precision=lax.Precision.HIGHEST)
    small = gram + train_count * jnp.eye(train_count, dtype=jnp.float32)
    small_inverse = inverse_factor(small)
    solved_all = train_count * mm(small_inverse.T, mm(small_inverse, prior_solved_t.T))
    solved_all = solved_all.astype(jnp.bfloat16)
    row_start = lax.axis_index("ex") * local_count
    solved = lax.dynamic_slice_in_dim(solved_all, row_start, local_count, 0)
    inverse_root = 1.0 / math.sqrt(feat_dim)
    block_probes = gather_rows(probes.astype(jnp.float32), "ex")
    return mm(block_probes, solved.astype(jnp.float32).T) * inverse_root


def solution(mesh):
    return jax.shard_map(
        per_device,
        mesh=mesh,
        in_specs=(
            P("ex", None, "param"),
            P("ex", None, "param"),
            P("param", None),
            P("param", None),
            P("ex", "param"),
            P(("param", "ex"), None),
        ),
        out_specs=P("param", "ex"),
        check_vma=False,
    )
```

```python
import functools
import math

import jax
import jax.numpy as jnp
from jax import lax
from jax.experimental import pallas as pl
from jax.experimental.pallas import tpu as pltpu
from jax.sharding import PartitionSpec as P


def _pick(row, index):
    lane = lax.broadcasted_iota(jnp.int32, row.shape, 1)
    return jnp.sum(jnp.where(lane == index, row, 0.0), axis=1, keepdims=True)


def _inverse_factor_kernel(width, a_ref, w_ref, s_ref):
    n = a_ref.shape[0]
    s_ref[...] = a_ref[...]
    rows = lax.broadcasted_iota(jnp.int32, (n, n), 0)
    cols = lax.broadcasted_iota(jnp.int32, (n, n), 1)
    w_ref[...] = jnp.where(rows == cols, 1.0, 0.0).astype(jnp.float32)
    segment = 32 if n % 32 == 0 else 8
    for group in range(n // segment):
        low = group * segment

        def step(t, carry):
            j = low + width * t
            pivots = [s_ref[pl.ds(j + m, 1), :] for m in range(width)]
            inverses = [w_ref[pl.ds(j + m, 1), :] for m in range(width)]
            block = [[None] * width for _ in range(width)]
            for m in range(width):
                for l in range(m + 1):
                    block[m][l] = _pick(pivots[m], j + l)
                    block[l][m] = block[m][l]
            coeffs = [[1.0 if l == m else 0.0 for l in range(width)] for m in range(width)]
            for m in range(width):
                scale = 1.0 / jnp.sqrt(block[m][m])
                block[m] = [b * scale for b in block[m]]
                coeffs[m] = [c * scale for c in coeffs[m]]
                for q in range(m + 1, width):
                    factor = block[q][m] * scale
                    block[q] = [bq - factor * bm for bq, bm in zip(block[q], block[m])]
                    coeffs[q] = [cq - factor * cm for cq, cm in zip(coeffs[q], coeffs[m])]
            new_pivots, new_inverses = [], []
            for m in range(width):
                p = pivots[0] * coeffs[m][0]
                v = inverses[0] * coeffs[m][0]
                for l in range(1, m + 1):
                    p = p + pivots[l] * coeffs[m][l]
                    v = v + inverses[l] * coeffs[m][l]
                new_pivots.append(p)
                new_inverses.append(v)
            rest = s_ref[low:, :]
            lanes = lax.broadcasted_iota(jnp.int32, rest.shape, 1)
            columns = [jnp.sum(jnp.where(lanes == j + l, rest, 0.0), axis=1, keepdims=True) for l in range(width)]
            below = lax.broadcasted_iota(jnp.int32, (n - low, 1), 0) + low
            keep = below >= j + width
            new_rest = rest
            new_inv = w_ref[low:, :]
            for m in range(width):
                f = columns[0] * coeffs[m][0]
                for l in range(1, m + 1):
                    f = f + columns[l] * coeffs[m][l]
                f = jnp.where(keep, f, 0.0)
                new_rest = new_rest - f * new_pivots[m]
                new_inv = new_inv - f * new_inverses[m]
            s_ref[low:, :] = new_rest
            w_ref[low:, :] = new_inv
            for m in range(width):
                s_ref[pl.ds(j + m, 1), :] = new_pivots[m]
                w_ref[pl.ds(j + m, 1), :] = new_inverses[m]
            return carry

        lax.fori_loop(0, segment // width, step, 0)


def inverse_factor(block, width=4):
    n = block.shape[0]
    return pl.pallas_call(
        functools.partial(_inverse_factor_kernel, width),
        out_shape=jax.ShapeDtypeStruct((n, n), jnp.float32),
        in_specs=[pl.BlockSpec(memory_space=pltpu.VMEM)],
        out_specs=pl.BlockSpec(memory_space=pltpu.VMEM),
        scratch_shapes=[pltpu.VMEM((n, n), jnp.float32)],
    )(block)


def outer_terms(factors, in_width):
    first = factors[:, :in_width]
    second = factors[:, in_width:]
    product = jnp.einsum("eol,eil->eoi", second, first, precision=lax.Precision.HIGHEST)
    return product.reshape(product.shape[0], -1)


def spd_solve(matrix, rhs_t):
    lower_factor = jnp.linalg.cholesky(matrix)
    halfway = lax.linalg.triangular_solve(lower_factor, rhs_t, left_side=True, lower=True)
    return lax.linalg.triangular_solve(
        lower_factor, halfway, left_side=True, lower=True, transpose_a=True
    )


def mm(a, b):
    return jnp.dot(a, b, precision=lax.Precision.HIGHEST, preferred_element_type=jnp.float32)


def blocked_cholesky(matrix, block):
    count = matrix.shape[0] // block
    inverses, panels = [], []
    trailing = matrix
    for k in range(count):
        inverse = inverse_factor(trailing[:block, :block])
        inverses.append(inverse)
        if k + 1 < count:
            panel = mm(trailing[block:, :block], inverse.T)
            panels.append(panel)
            trailing = trailing[block:, block:] - mm(panel, panel.T)
    return inverses, panels


def blocked_solve(inverses, panels, rhs, block):
    count = len(inverses)
    parts = []
    rest = rhs
    for k in range(count):
        part = mm(inverses[k], rest[:block])
        parts.append(part)
        if k + 1 < count:
            rest = rest[block:] - mm(panels[k], part)
    done = None
    for k in reversed(range(count)):
        target = parts[k]
        if done is not None:
            target = target - mm(panels[k].T, done)
        part = mm(inverses[k].T, target)
        done = part if done is None else jnp.concatenate((part, done), axis=0)
    return done


def gather_rows(block_rows, axis_name):
    count = lax.axis_size(axis_name)
    rows = block_rows.shape[0]
    padded = jnp.zeros((count * rows,) + block_rows.shape[1:], block_rows.dtype)
    padded = lax.dynamic_update_slice_in_dim(padded, block_rows, lax.axis_index(axis_name) * rows, 0)
    return lax.psum(padded, axis_name)


def gather_prior(prior):
    n_ex = lax.axis_size("ex")
    n_par = lax.axis_size("param")
    rows, cols = prior.shape
    blocks = lax.all_gather(prior, ("ex", "param"), axis=0, tiled=False)
    return jnp.concatenate(
        [jnp.concatenate([blocks[e * n_par + p] for p in range(n_par)], axis=1) for e in range(n_ex)], axis=0
    )


def per_device(activations, out_grads, proj_in, proj_out, prior, probes):
    full_prior = gather_prior(prior)
    tokens = activations.shape[1]
    in_width = proj_in.shape[1]
    factor_in = jnp.einsum("eld,dk->ekl", activations, proj_in, preferred_element_type=jnp.float32)
    factor_out = jnp.einsum("eld,dk->ekl", out_grads, proj_out, preferred_element_type=jnp.float32)
    factors = jnp.concatenate((factor_in, factor_out), axis=1)
    factors = lax.psum(factors, "param")
    summed = outer_terms(factors, in_width)
    features = (summed * (1.0 / math.sqrt(tokens))).astype(jnp.bfloat16)
    local_count, feat_dim = features.shape
    all_features = gather_rows(features.astype(jnp.float32), "ex")
    train_count = all_features.shape[0]
    block = 128 if feat_dim % 128 == 0 else feat_dim
    inverses, panels = blocked_cholesky(full_prior, block)
    later = inverses[len(inverses) // 2][:1, :1]
    prior_solved_t = blocked_solve(inverses, panels, all_features.T + 0.0 * later, block)
    gram = jnp.dot(all_features, prior_solved_t, precision=lax.Precision.HIGHEST)
    small = gram + train_count * jnp.eye(train_count, dtype=jnp.float32)
    small_inverse = inverse_factor(small)
    solved_all = train_count * mm(small_inverse.T, mm(small_inverse, prior_solved_t.T))
    solved_all = solved_all.astype(jnp.bfloat16)
    row_start = lax.axis_index("ex") * local_count
    solved = lax.dynamic_slice_in_dim(solved_all, row_start, local_count, 0)
    inverse_root = 1.0 / math.sqrt(feat_dim)
    block_probes = gather_rows(probes.astype(jnp.float32), "ex")
    return mm(block_probes, solved.astype(jnp.float32).T) * inverse_root


def solution(mesh):
    return jax.shard_map(
        per_device,
        mesh=mesh,
        in_specs=(
            P("ex", None, "param"),
            P("ex", None, "param"),
            P("param", None),
            P("param", None),
            P("ex", "param"),
            P(("param", "ex"), None),
        ),
        out_specs=P("param", "ex"),
        check_vma=False,
    )
```

```python
import functools
import math

import jax
import jax.numpy as jnp
from jax import lax
from jax.experimental import pallas as pl
from jax.experimental.pallas import tpu as pltpu
from jax.sharding import PartitionSpec as P


def _pick(row, index):
    lane = lax.broadcasted_iota(jnp.int32, row.shape, 1)
    return jnp.sum(jnp.where(lane == index, row, 0.0), axis=1, keepdims=True)


def _inverse_factor_kernel(width, a_ref, w_ref, s_ref):
    n = a_ref.shape[0]
    s_ref[...] = a_ref[...]
    rows = lax.broadcasted_iota(jnp.int32, (n, n), 0)
    cols = lax.broadcasted_iota(jnp.int32, (n, n), 1)
    w_ref[...] = jnp.where(rows == cols, 1.0, 0.0).astype(jnp.float32)
    segment = 16 if n % 16 == 0 else 8
    for group in range(n // segment):
        low = group * segment

        def step(t, carry):
            j = low + width * t
            pivots = [s_ref[pl.ds(j + m, 1), :] for m in range(width)]
            inverses = [w_ref[pl.ds(j + m, 1), :] for m in range(width)]
            block = [[None] * width for _ in range(width)]
            for m in range(width):
                for l in range(m + 1):
                    block[m][l] = _pick(pivots[m], j + l)
                    block[l][m] = block[m][l]
            coeffs = [[1.0 if l == m else 0.0 for l in range(width)] for m in range(width)]
            for m in range(width):
                scale = 1.0 / jnp.sqrt(block[m][m])
                block[m] = [b * scale for b in block[m]]
                coeffs[m] = [c * scale for c in coeffs[m]]
                for q in range(m + 1, width):
                    factor = block[q][m] * scale
                    block[q] = [bq - factor * bm for bq, bm in zip(block[q], block[m])]
                    coeffs[q] = [cq - factor * cm for cq, cm in zip(coeffs[q], coeffs[m])]
            new_pivots, new_inverses = [], []
            for m in range(width):
                p = pivots[0] * coeffs[m][0]
                v = inverses[0] * coeffs[m][0]
                for l in range(1, m + 1):
                    p = p + pivots[l] * coeffs[m][l]
                    v = v + inverses[l] * coeffs[m][l]
                new_pivots.append(p)
                new_inverses.append(v)
            rest = s_ref[low:, :]
            lanes = lax.broadcasted_iota(jnp.int32, rest.shape, 1)
            columns = [jnp.sum(jnp.where(lanes == j + l, rest, 0.0), axis=1, keepdims=True) for l in range(width)]
            below = lax.broadcasted_iota(jnp.int32, (n - low, 1), 0) + low
            keep = below >= j + width
            new_rest = rest
            new_inv = w_ref[low:, :]
            for m in range(width):
                f = columns[0] * coeffs[m][0]
                for l in range(1, m + 1):
                    f = f + columns[l] * coeffs[m][l]
                f = jnp.where(keep, f, 0.0)
                new_rest = new_rest - f * new_pivots[m]
                new_inv = new_inv - f * new_inverses[m]
            s_ref[low:, :] = new_rest
            w_ref[low:, :] = new_inv
            for m in range(width):
                s_ref[pl.ds(j + m, 1), :] = new_pivots[m]
                w_ref[pl.ds(j + m, 1), :] = new_inverses[m]
            return carry

        lax.fori_loop(0, segment // width, step, 0)


def inverse_factor(block, width=4):
    n = block.shape[0]
    return pl.pallas_call(
        functools.partial(_inverse_factor_kernel, width),
        out_shape=jax.ShapeDtypeStruct((n, n), jnp.float32),
        in_specs=[pl.BlockSpec(memory_space=pltpu.VMEM)],
        out_specs=pl.BlockSpec(memory_space=pltpu.VMEM),
        scratch_shapes=[pltpu.VMEM((n, n), jnp.float32)],
    )(block)


def outer_terms(factors, in_width):
    first = factors[:, :in_width]
    second = factors[:, in_width:]
    product = jnp.einsum("eol,eil->eoi", second, first, precision=lax.Precision.HIGHEST)
    return product.reshape(product.shape[0], -1)


def spd_solve(matrix, rhs_t):
    lower_factor = jnp.linalg.cholesky(matrix)
    halfway = lax.linalg.triangular_solve(lower_factor, rhs_t, left_side=True, lower=True)
    return lax.linalg.triangular_solve(
        lower_factor, halfway, left_side=True, lower=True, transpose_a=True
    )


def mm(a, b):
    return jnp.dot(a, b, precision=lax.Precision.HIGHEST, preferred_element_type=jnp.float32)


def blocked_cholesky(matrix, block):
    count = matrix.shape[0] // block
    inverses, panels = [], []
    trailing = matrix
    for k in range(count):
        inverse = inverse_factor(trailing[:block, :block])
        inverses.append(inverse)
        if k + 1 < count:
            panel = mm(trailing[block:, :block], inverse.T)
            panels.append(panel)
            trailing = trailing[block:, block:] - mm(panel, panel.T)
    return inverses, panels


def blocked_solve(inverses, panels, rhs, block):
    count = len(inverses)
    parts = []
    rest = rhs
    for k in range(count):
        part = mm(inverses[k], rest[:block])
        parts.append(part)
        if k + 1 < count:
            rest = rest[block:] - mm(panels[k], part)
    done = None
    for k in reversed(range(count)):
        target = parts[k]
        if done is not None:
            target = target - mm(panels[k].T, done)
        part = mm(inverses[k].T, target)
        done = part if done is None else jnp.concatenate((part, done), axis=0)
    return done


def gather_rows(block_rows, axis_name):
    count = lax.axis_size(axis_name)
    rows = block_rows.shape[0]
    padded = jnp.zeros((count * rows,) + block_rows.shape[1:], block_rows.dtype)
    padded = lax.dynamic_update_slice_in_dim(padded, block_rows, lax.axis_index(axis_name) * rows, 0)
    return lax.psum(padded, axis_name)


def gather_prior(prior):
    n_ex = lax.axis_size("ex")
    n_par = lax.axis_size("param")
    rows, cols = prior.shape
    blocks = lax.all_gather(prior, ("ex", "param"), axis=0, tiled=False)
    return jnp.concatenate(
        [jnp.concatenate([blocks[e * n_par + p] for p in range(n_par)], axis=1) for e in range(n_ex)], axis=0
    )


def per_device(activations, out_grads, proj_in, proj_out, prior, probes):
    full_prior = gather_prior(prior)
    tokens = activations.shape[1]
    in_width = proj_in.shape[1]
    factor_in = jnp.einsum("eld,dk->ekl", activations, proj_in, preferred_element_type=jnp.float32)
    factor_out = jnp.einsum("eld,dk->ekl", out_grads, proj_out, preferred_element_type=jnp.float32)
    factors = jnp.concatenate((factor_in, factor_out), axis=1)
    factors = lax.psum(factors, "param")
    summed = outer_terms(factors, in_width)
    features = (summed * (1.0 / math.sqrt(tokens))).astype(jnp.bfloat16)
    local_count, feat_dim = features.shape
    all_features = gather_rows(features.astype(jnp.float32), "ex")
    train_count = all_features.shape[0]
    block = 128 if feat_dim % 128 == 0 else feat_dim
    inverses, panels = blocked_cholesky(full_prior, block)
    later = inverses[len(inverses) // 2][:1, :1]
    prior_solved_t = blocked_solve(inverses, panels, all_features.T + 0.0 * later, block)
    gram = jnp.dot(all_features, prior_solved_t, precision=lax.Precision.HIGHEST)
    small = gram + train_count * jnp.eye(train_count, dtype=jnp.float32)
    small_inverse = inverse_factor(small)
    solved_all = train_count * mm(small_inverse.T, mm(small_inverse, prior_solved_t.T))
    solved_all = solved_all.astype(jnp.bfloat16)
    row_start = lax.axis_index("ex") * local_count
    solved = lax.dynamic_slice_in_dim(solved_all, row_start, local_count, 0)
    inverse_root = 1.0 / math.sqrt(feat_dim)
    block_probes = gather_rows(probes.astype(jnp.float32), "ex")
    return mm(block_probes, solved.astype(jnp.float32).T) * inverse_root


def solution(mesh):
    return jax.shard_map(
        per_device,
        mesh=mesh,
        in_specs=(
            P("ex", None, "param"),
            P("ex", None, "param"),
            P("param", None),
            P("param", None),
            P("ex", "param"),
            P(("param", "ex"), None),
        ),
        out_specs=P("param", "ex"),
        check_vma=False,
    )
```

```python
import functools
import math

import jax
import jax.numpy as jnp
from jax import lax
from jax.experimental import pallas as pl
from jax.experimental.pallas import tpu as pltpu
from jax.sharding import PartitionSpec as P


def _pick(row, index):
    lane = lax.broadcasted_iota(jnp.int32, row.shape, 1)
    return jnp.sum(jnp.where(lane == index, row, 0.0), axis=1, keepdims=True)


def _inverse_factor_kernel(width, a_ref, w_ref, s_ref):
    n = a_ref.shape[0]
    s_ref[...] = a_ref[...]
    rows = lax.broadcasted_iota(jnp.int32, (n, n), 0)
    cols = lax.broadcasted_iota(jnp.int32, (n, n), 1)
    w_ref[...] = jnp.where(rows == cols, 1.0, 0.0).astype(jnp.float32)
    segment = 16 if n % 16 == 0 else 8
    for group in range(n // segment):
        low = group * segment

        def step(t, carry):
            j = low + width * t
            pivots = [s_ref[pl.ds(j + m, 1), :] for m in range(width)]
            inverses = [w_ref[pl.ds(j + m, 1), :] for m in range(width)]
            block = [[None] * width for _ in range(width)]
            for m in range(width):
                for l in range(m + 1):
                    block[m][l] = _pick(pivots[m], j + l)
                    block[l][m] = block[m][l]
            coeffs = [[1.0 if l == m else 0.0 for l in range(width)] for m in range(width)]
            for m in range(width):
                scale = 1.0 / jnp.sqrt(block[m][m])
                block[m] = [b * scale for b in block[m]]
                coeffs[m] = [c * scale for c in coeffs[m]]
                for q in range(m + 1, width):
                    factor = block[q][m] * scale
                    block[q] = [bq - factor * bm for bq, bm in zip(block[q], block[m])]
                    coeffs[q] = [cq - factor * cm for cq, cm in zip(coeffs[q], coeffs[m])]
            new_pivots, new_inverses = [], []
            for m in range(width):
                p = pivots[0] * coeffs[m][0]
                v = inverses[0] * coeffs[m][0]
                for l in range(1, m + 1):
                    p = p + pivots[l] * coeffs[m][l]
                    v = v + inverses[l] * coeffs[m][l]
                new_pivots.append(p)
                new_inverses.append(v)
            rest = s_ref[low:, :]
            lanes = lax.broadcasted_iota(jnp.int32, rest.shape, 1)
            columns = [jnp.sum(jnp.where(lanes == j + l, rest, 0.0), axis=1, keepdims=True) for l in range(width)]
            below = lax.broadcasted_iota(jnp.int32, (n - low, 1), 0) + low
            keep = below >= j + width
            new_rest = rest
            new_inv = w_ref[low:, :]
            for m in range(width):
                f = columns[0] * coeffs[m][0]
                for l in range(1, m + 1):
                    f = f + columns[l] * coeffs[m][l]
                f = jnp.where(keep, f, 0.0)
                new_rest = new_rest - f * new_pivots[m]
                new_inv = new_inv - f * new_inverses[m]
            s_ref[low:, :] = new_rest
            w_ref[low:, :] = new_inv
            for m in range(width):
                s_ref[pl.ds(j + m, 1), :] = new_pivots[m]
                w_ref[pl.ds(j + m, 1), :] = new_inverses[m]
            return carry

        lax.fori_loop(0, segment // width, step, 0)


def inverse_factor(block, width=4):
    n = block.shape[0]
    return pl.pallas_call(
        functools.partial(_inverse_factor_kernel, width),
        out_shape=jax.ShapeDtypeStruct((n, n), jnp.float32),
        in_specs=[pl.BlockSpec(memory_space=pltpu.VMEM)],
        out_specs=pl.BlockSpec(memory_space=pltpu.VMEM),
        scratch_shapes=[pltpu.VMEM((n, n), jnp.float32)],
    )(block)


def outer_terms(factors, in_width):
    first = factors[:, :in_width]
    second = factors[:, in_width:]
    product = jnp.einsum("eol,eil->eoi", second, first, precision=lax.Precision.HIGHEST)
    return product.reshape(product.shape[0], -1)


def spd_solve(matrix, rhs_t):
    lower_factor = jnp.linalg.cholesky(matrix)
    halfway = lax.linalg.triangular_solve(lower_factor, rhs_t, left_side=True, lower=True)
    return lax.linalg.triangular_solve(
        lower_factor, halfway, left_side=True, lower=True, transpose_a=True
    )


def mm(a, b):
    return jnp.dot(a, b, precision=lax.Precision.HIGHEST, preferred_element_type=jnp.float32)


def blocked_cholesky(matrix, block):
    count = matrix.shape[0] // block
    inverses, panels = [], []
    trailing = matrix
    for k in range(count):
        inverse = inverse_factor(trailing[:block, :block])
        inverses.append(inverse)
        if k + 1 < count:
            panel = mm(trailing[block:, :block], inverse.T)
            panels.append(panel)
            trailing = trailing[block:, block:] - mm(panel, panel.T)
    return inverses, panels


def blocked_solve(inverses, panels, rhs, block):
    count = len(inverses)
    parts = []
    rest = rhs
    for k in range(count):
        part = mm(inverses[k], rest[:block])
        parts.append(part)
        if k + 1 < count:
            rest = rest[block:] - mm(panels[k], part)
    done = jnp.zeros((count * block,) + rhs.shape[1:], jnp.float32)
    for k in reversed(range(count)):
        target = parts[k]
        if k + 1 < count:
            target = target - mm(panels[k].T, done[(k + 1) * block:])
        done = lax.dynamic_update_slice_in_dim(done, mm(inverses[k].T, target), k * block, 0)
    return done


def gather_rows(block_rows, axis_name):
    count = lax.axis_size(axis_name)
    rows = block_rows.shape[0]
    padded = jnp.zeros((count * rows,) + block_rows.shape[1:], block_rows.dtype)
    padded = lax.dynamic_update_slice_in_dim(padded, block_rows, lax.axis_index(axis_name) * rows, 0)
    return lax.psum(padded, axis_name)


def gather_prior(prior):
    n_ex = lax.axis_size("ex")
    n_par = lax.axis_size("param")
    rows, cols = prior.shape
    blocks = lax.all_gather(prior, ("ex", "param"), axis=0, tiled=False)
    return jnp.concatenate(
        [jnp.concatenate([blocks[e * n_par + p] for p in range(n_par)], axis=1) for e in range(n_ex)], axis=0
    )


def per_device(activations, out_grads, proj_in, proj_out, prior, probes):
    full_prior = gather_prior(prior)
    tokens = activations.shape[1]
    in_width = proj_in.shape[1]
    factor_in = jnp.einsum("eld,dk->ekl", activations, proj_in, preferred_element_type=jnp.float32)
    factor_out = jnp.einsum("eld,dk->ekl", out_grads, proj_out, preferred_element_type=jnp.float32)
    factors = jnp.concatenate((factor_in, factor_out), axis=1)
    factors = lax.psum(factors, "param")
    summed = outer_terms(factors, in_width)
    features = (summed * (1.0 / math.sqrt(tokens))).astype(jnp.bfloat16)
    local_count, feat_dim = features.shape
    all_features = gather_rows(features.astype(jnp.float32), "ex")
    train_count = all_features.shape[0]
    block = 128 if feat_dim % 128 == 0 else feat_dim
    inverses, panels = blocked_cholesky(full_prior, block)
    later = inverses[len(inverses) // 2][:1, :1]
    prior_solved_t = blocked_solve(inverses, panels, all_features.T + 0.0 * later, block)
    gram = jnp.dot(all_features, prior_solved_t, precision=lax.Precision.HIGHEST)
    small = gram + train_count * jnp.eye(train_count, dtype=jnp.float32)
    small_inverse = inverse_factor(small)
    solved_all = train_count * mm(small_inverse.T, mm(small_inverse, prior_solved_t.T))
    solved_all = solved_all.astype(jnp.bfloat16)
    row_start = lax.axis_index("ex") * local_count
    solved = lax.dynamic_slice_in_dim(solved_all, row_start, local_count, 0)
    inverse_root = 1.0 / math.sqrt(feat_dim)
    block_probes = gather_rows(probes.astype(jnp.float32), "ex")
    return mm(block_probes, solved.astype(jnp.float32).T) * inverse_root


def solution(mesh):
    return jax.shard_map(
        per_device,
        mesh=mesh,
        in_specs=(
            P("ex", None, "param"),
            P("ex", None, "param"),
            P("param", None),
            P("param", None),
            P("ex", "param"),
            P(("param", "ex"), None),
        ),
        out_specs=P("param", "ex"),
        check_vma=False,
    )
```
